128 devices in a mesh: front: 4 (over z), row: 4 (over x_lo, core), col: 8 (over x_hi, y).
Axes of the slice: x: 4 (x_hi: 2, x_lo: 2; x = x_hi * 2 + x_lo), y: 4, z: 4, core: 2. Of those that a mesh axis runs over, the one named last changes fastest.
Arguments:
- front_orig: float32 [4, 8192, 8192], P('front', 'row', 'col'), may hold values from -6 to 6
- children: float32 [4, 2048, 2048], P('front', 'row', 'col'), may hold values from -6 to 6
- parent_of: int32 [4], P('front'), may hold values from 0 to 3, as said below
- child_map: int32 [4, 8], P('front'), may hold values from 0 to 31, as said below
- block_mask: int32 [4, 32, 32], P('front'), may hold values 0 or 1
- pivot: int32 [4, 32], P('front'), may hold values from 0 to 31, each once within a row
- diag_inverse: float32 [4, 2, 512, 512], P('front'), may hold values from -0.01171875 to 0.01171875
Outputs:
- factored: float32 [4, 8192, 8192], P('front', 'row', 'col')
The draws below stay inside these ranges and needn't reach their ends.
Inputs may be any that keep to these rules, and one draw needn't show every extreme that they name: `parent_of`: each front is the parent of exactly one child update. Each row of child_map is strictly increasing.
All inputs are finite; a program needn't handle non-finite values. No bound on the sum of `block_mask` on one device may be relied on, other than what follows from the above.
Results may differ from the reference program's by a relative error of at most 0.00011.
Values sent between devices are 32-bit elements; how exact they have to be, the bound alone decides.
No kernel may reach another device: no remote copies, remote signals or barrier semaphores. Data moves between devices by JAX's collectives and lax.ppermute only.
A program may use at most 128 MiB of HBM per device.

```python
import jax
import jax.numpy as jnp
from jax import lax

BS = 256
F = 8192
PANELS = 2
KIDS = 1
NB = 32
CB = 8
CU = 2048
PW = 512
NFR = 4
NCH = 4
N_ROW = 4


def draw_parent_of(key, part):
    owners = jnp.repeat(jnp.arange(NFR, dtype=jnp.int32), KIDS)
    owners = jax.random.permutation(key, owners).astype(jnp.int32)
    target = NFR // 2 * KIDS
    found = jnp.argmax((owners == 0).astype(jnp.int32)).astype(jnp.int32)
    moved = owners[target]
    owners = owners.at[found].set(moved).at[target].set(0)
    return owners.astype(jnp.int32)


def draw_child_map(key, part):

    def one_child(index):
        picks = jax.random.permutation(jax.random.fold_in(key, index), NB)[:CB]
        return jnp.sort(picks.astype(jnp.int32))
    rows_all = jax.vmap(one_child)(jnp.arange(NCH, dtype=jnp.int32))
    low_span = NB // N_ROW
    low_picks = jax.random.permutation(jax.random.fold_in(key, 7919), low_span - 1)[:CB // 2].astype(jnp.int32) + 1
    high_picks = jax.random.permutation(jax.random.fold_in(key, 7927), NB - low_span - 1)[:CB // 2 - 2].astype(jnp.int32) + low_span
    ends = jnp.array([0, NB - 1], jnp.int32)
    first_row = jnp.sort(jnp.concatenate([ends, low_picks, high_picks]))
    return rows_all.at[0].set(first_row).astype(jnp.int32)


def plant(drawn, stream_key, least, top_value):
    extent = drawn.shape
    spot = [jax.random.randint(jax.random.fold_in(stream_key, axis), (), 0, extent[axis]) for axis in range(len(extent))]
    drawn = drawn.at[tuple(spot)].set(least)
    longest = extent.index(max(extent))
    spot[longest] = (spot[longest] + 1) % extent[longest]
    return drawn.at[tuple(spot)].set(top_value)


def level_of(stream_key, shape, split, low, top_value):
    loudness = 1.0
    for dim, blocks in split:
        steps = jax.random.uniform(jax.random.fold_in(jax.random.fold_in(stream_key, 6), dim), (blocks,), jnp.float32, low / len(split), top_value / len(split))
        loudness = loudness * jnp.repeat(jnp.exp(steps), shape[dim] // blocks).reshape((-1,) + (1,) * (len(shape) - 1 - dim))
    return loudness


def gaussian(own_key, dims, width, limit, cuts=(), held_as=jnp.bfloat16):
    values = width * jax.random.normal(own_key, dims, jnp.float32)
    if cuts:
        values = values * level_of(own_key, dims, cuts, -0.22, 0.18)
    return jnp.clip(values, -limit, limit).astype(held_as)


def setup_inputs(seed: int = 0) -> dict:
    keys = jax.random.split(jax.random.key(seed), 8)
    return {
        "front_orig": gaussian(keys[0], (NFR, F, F), 1.0, 6.0, ((0, 4), (1, 4), (2, 8)), jnp.float32),
        "children": gaussian(keys[1], (NCH, CU, CU), 1.0, 6.0, ((0, 4), (1, 4), (2, 8)), jnp.float32),
        "parent_of": draw_parent_of(jax.random.fold_in(keys[7], 71), 0),
        "child_map": draw_child_map(jax.random.fold_in(keys[7], 71), 0),
        "block_mask": plant((jax.random.randint(keys[4], (NFR, NB, NB), 0, 4) < 3).astype(jnp.int32), jax.random.fold_in(keys[4], 1), 0, 1),
        "pivot": jax.vmap(lambda own: jax.random.permutation(own, NB))(jax.random.split(keys[5], NFR)).reshape((NFR, NB)).astype(jnp.int32),
        "diag_inverse": gaussian(keys[6], (NFR, PANELS, PW, PW), (PW * PW) ** -0.5, 0.01171875, ((0, 4),), jnp.float32),
    }


HIGH = lax.Precision.HIGHEST


def place(update, mapping):
    nblocks = F // BS
    tiles = update.reshape(CB, BS, CB, BS).transpose(0, 2, 1, 3)
    grid = jnp.zeros((nblocks, nblocks, BS, BS), jnp.float32).at[mapping[:, None], mapping[None, :]].set(tiles)
    return grid.transpose(0, 2, 1, 3).reshape(F, F)


def spread(grid):
    return jnp.repeat(jnp.repeat(grid, BS, axis=0), BS, axis=1)


def reference(front_orig, children, parent_of, child_map, block_mask, pivot, diag_inverse):
    nblocks = F // BS

    def add_child(total, item):
        update, owner, mapping = item
        placed = place(update, mapping)
        return total.at[owner].add(placed), None

    extended, _ = lax.scan(add_child, jnp.zeros((NFR, F, F), jnp.float32), (children, parent_of, child_map))
    results = []
    ranks = jnp.arange(nblocks, dtype=jnp.int32)
    for front in range(NFR):
        mask = block_mask[front].astype(jnp.float32)
        matrix = spread(mask) * (front_orig[front] + extended[front])
        order = pivot[front]
        position = jnp.sum(jnp.where(order[:, None] == ranks[None, :], ranks[:, None], 0), axis=0).astype(jnp.int32)
        for step in range(PANELS):
            alive = (position >= 2 * step + 2).astype(jnp.float32)
            live = jnp.repeat(alive, BS)
            first = order[2 * step]
            second = order[2 * step + 1]
            column_panel = jnp.concatenate([lax.dynamic_slice_in_dim(matrix, first * BS, BS, 1), lax.dynamic_slice_in_dim(matrix, second * BS, BS, 1)], axis=1)
            row_panel = jnp.concatenate([lax.dynamic_slice_in_dim(matrix, first * BS, BS, 0), lax.dynamic_slice_in_dim(matrix, second * BS, BS, 0)], axis=0)
            lower = jnp.dot(column_panel, diag_inverse[front, step], precision=HIGH, preferred_element_type=jnp.float32)
            update = jnp.dot(lower * live[:, None], row_panel, precision=HIGH, preferred_element_type=jnp.float32)
            matrix = matrix - update * spread(mask * alive[:, None] * alive[None, :])
            for half, chosen in enumerate((first, second)):
                current = lax.dynamic_slice_in_dim(matrix, chosen * BS, BS, 1)
                written = jnp.where(live[:, None] > 0, lower[:, half * BS:(half + 1) * BS], current)
                matrix = lax.dynamic_update_slice_in_dim(matrix, written, chosen * BS, 1)
        results.append(matrix)
    return jnp.stack(results)
```

```python
import jax
import jax.numpy as jnp
from jax import lax
from jax.sharding import PartitionSpec as P

BS = 256


HIGH = lax.Precision.HIGHEST


def dot(a, b):
    return jnp.dot(a, b, precision=HIGH, preferred_element_type=jnp.float32)


def body(front_orig, children, parent_of, child_map, block_mask, pivot, diag_inverse):
    row_count = lax.axis_size("row")
    col_count = lax.axis_size("col")
    front_count = lax.axis_size("front")
    row_id = lax.axis_index("row")
    col_id = lax.axis_index("col")
    front_id = lax.axis_index("front")
    matrix_in = front_orig[0]
    loc_rows, loc_cols = matrix_in.shape
    row_blocks = loc_rows // BS
    col_blocks = loc_cols // BS
    kid_rows = children.shape[1] // BS
    kid_cols = children.shape[2] // BS

    def spread(grid):
        r, c = grid.shape
        return jnp.broadcast_to(grid[:, None, :, None], (r, BS, c, BS)).reshape(r * BS, c * BS)

    piece = children[0]
    tags = jnp.concatenate([parent_of, child_map[0]])
    best_piece = jnp.where(tags[0] == front_id, piece, jnp.zeros_like(piece))
    best_tags = jnp.where(tags[0] == front_id, tags, jnp.zeros_like(tags))
    for shift in range(1, front_count):
        perm = [(i, (i + shift) % front_count) for i in range(front_count)]
        got_piece = lax.ppermute(piece, "front", perm)
        got_tags = lax.ppermute(tags, "front", perm)
        hit = got_tags[0] == front_id
        best_piece = jnp.where(hit, got_piece, best_piece)
        best_tags = jnp.where(hit, got_tags, best_tags)
    own_map = best_tags[1:]
    child_blocks = own_map.shape[0]
    block_ranks = jnp.arange(child_blocks, dtype=jnp.int32)

    def locate(first, width):
        target = first + jnp.arange(width, dtype=jnp.int32)
        matches = own_map[:, None] == target[None, :]
        source = jnp.sum(jnp.where(matches, block_ranks[:, None], 0), axis=0)
        return source, jnp.any(matches, axis=0)

    row_src, row_has = locate(row_id * row_blocks, row_blocks)
    col_src, col_has = locate(col_id * col_blocks, col_blocks)
    gathered = lax.all_gather(best_piece, ("row", "col"), axis=0, tiled=False)
    child_tiles = gathered.reshape(row_count, col_count, kid_rows, BS, kid_cols, BS)
    picked = child_tiles[
        (row_src // kid_rows)[:, None],
        (col_src // kid_cols)[None, :],
        (row_src % kid_rows)[:, None],
        :,
        (col_src % kid_cols)[None, :],
        :,
    ]
    keep = row_has[:, None] & col_has[None, :]
    picked = jnp.where(keep[:, :, None, None], picked, 0.0)
    extended = picked.transpose(0, 2, 1, 3).reshape(loc_rows, loc_cols)

    mask_all = block_mask[0].astype(jnp.float32)
    mask_local = lax.dynamic_slice(
        mask_all, (row_id * row_blocks, col_id * col_blocks), (row_blocks, col_blocks)
    )
    assembled = spread(mask_local) * (matrix_in + extended)

    order = pivot[0]
    nblocks = order.shape[0]
    ranks = jnp.arange(nblocks, dtype=jnp.int32)
    position = jnp.sum(jnp.where(order[:, None] == ranks[None, :], ranks[:, None], 0), axis=0)
    alive0 = (position >= 2).astype(jnp.float32)
    alive1 = (position >= 4).astype(jnp.float32)
    piv = [order[k] for k in range(4)]

    col_parts = []
    for blk in piv:
        piece_c = lax.dynamic_slice_in_dim(assembled, (blk % col_blocks) * BS, BS, 1)
        col_parts.append(jnp.where(col_id == blk // col_blocks, piece_c, 0.0))
    col_panels = lax.psum(jnp.concatenate(col_parts, axis=1), "col")

    def rows_of(blk, cols):
        strip = lax.dynamic_slice_in_dim(cols, (blk % row_blocks) * BS, BS, 0)
        return jnp.where(row_id == blk // row_blocks, strip, 0.0)

    corner_x = jnp.concatenate([rows_of(piv[0], col_panels[:, 2 * BS:]), rows_of(piv[1], col_panels[:, 2 * BS:])], axis=0)
    corner_y = jnp.concatenate([rows_of(piv[2], col_panels[:, :2 * BS]), rows_of(piv[3], col_panels[:, :2 * BS])], axis=0)

    row_parts = [rows_of(blk, assembled) for blk in piv]
    row_payload = jnp.concatenate(row_parts + [jnp.concatenate([corner_x, corner_y], axis=1)], axis=0)
    row_payload = lax.psum(row_payload, "row")
    row_panels = row_payload[: 4 * BS]
    corner_x = row_payload[4 * BS:, : 2 * BS]
    corner_y = row_payload[4 * BS:, 2 * BS:]

    alive0_rows = jnp.repeat(lax.dynamic_slice_in_dim(alive0, row_id * row_blocks, row_blocks), BS)
    alive1_rows = jnp.repeat(lax.dynamic_slice_in_dim(alive1, row_id * row_blocks, row_blocks), BS)
    alive0_cb = lax.dynamic_slice_in_dim(alive0, col_id * col_blocks, col_blocks)
    alive1_cb = lax.dynamic_slice_in_dim(alive1, col_id * col_blocks, col_blocks)
    alive0_cols = jnp.repeat(alive0_cb, BS)
    alive1_cols = jnp.repeat(alive1_cb, BS)

    lower0 = dot(col_panels[:, : 2 * BS], diag_inverse[0, 0])
    w0 = lower0 * alive0_rows[:, None]
    mask_rows_p1q1 = lax.dynamic_slice_in_dim(
        jnp.stack([mask_all[:, piv[2]], mask_all[:, piv[3]]], axis=1), row_id * row_blocks, row_blocks, 0
    )
    cp1 = col_panels[:, 2 * BS:] - dot(w0, corner_x) * spread(mask_rows_p1q1)
    lower1 = dot(cp1, diag_inverse[0, 1])
    w1 = lower1 * alive1_rows[:, None]
    rp0 = row_panels[: 2 * BS]
    lower0_p1q1 = dot(corner_y, diag_inverse[0, 0])
    mask_p1q1_cols = lax.dynamic_slice_in_dim(
        jnp.stack([mask_all[piv[2]], mask_all[piv[3]]], axis=0), col_id * col_blocks, col_blocks, 1
    )
    rp1 = row_panels[2 * BS:] - dot(lower0_p1q1, rp0) * spread(mask_p1q1_cols * alive0_cb[None, :])

    lowers = jnp.concatenate([w0, w1], axis=1)
    uppers = jnp.concatenate([rp0 * alive0_cols[None, :], rp1 * alive1_cols[None, :]], axis=0)
    update = dot(lowers, uppers)
    fresh = assembled - update * spread(mask_local)

    replaced = [(piv[0], lower0[:, :BS], alive0_rows), (piv[1], lower0[:, BS:], alive0_rows),
                (piv[2], lower1[:, :BS], alive1_rows), (piv[3], lower1[:, BS:], alive1_rows)]
    for blk, values, live in replaced:
        slot = blk % col_blocks
        current = lax.dynamic_slice_in_dim(fresh, slot * BS, BS, 1)
        written = jnp.where((live[:, None] > 0) & (col_id == blk // col_blocks), values, current)
        fresh = lax.dynamic_update_slice_in_dim(fresh, written, slot * BS, 1)
    return fresh[None]


def solution(mesh):
    placed = (
        P("front", "row", "col"),
        P("front", "row", "col"),
        P("front"),
        P("front", None),
        P("front", None, None),
        P("front", None),
        P("front", None, None, None),
    )
    return jax.shard_map(
        body, mesh=mesh, in_specs=placed, out_specs=P("front", "row", "col"), check_vma=False
    )
```

```python
import jax
import jax.numpy as jnp
from jax import lax
from jax.sharding import PartitionSpec as P

BS = 256


HIGH = lax.Precision.HIGHEST


def dot(a, b):
    return jnp.dot(a, b, precision=HIGH, preferred_element_type=jnp.float32)


def body(front_orig, children, parent_of, child_map, block_mask, pivot, diag_inverse):
    row_count = lax.axis_size("row")
    col_count = lax.axis_size("col")
    front_count = lax.axis_size("front")
    row_id = lax.axis_index("row")
    col_id = lax.axis_index("col")
    front_id = lax.axis_index("front")
    matrix_in = front_orig[0]
    loc_rows, loc_cols = matrix_in.shape
    row_blocks = loc_rows // BS
    col_blocks = loc_cols // BS
    kid_rows = children.shape[1] // BS
    kid_cols = children.shape[2] // BS

    def spread(grid):
        r, c = grid.shape
        return jnp.broadcast_to(grid[:, None, :, None], (r, BS, c, BS)).reshape(r * BS, c * BS)

    piece = children[0]
    tags = jnp.concatenate([parent_of, child_map[0]])
    best_piece = jnp.where(tags[0] == front_id, piece, jnp.zeros_like(piece))
    best_tags = jnp.where(tags[0] == front_id, tags, jnp.zeros_like(tags))
    for shift in range(1, front_count):
        perm = [(i, (i + shift) % front_count) for i in range(front_count)]
        got_piece = lax.ppermute(piece, "front", perm)
        got_tags = lax.ppermute(tags, "front", perm)
        hit = got_tags[0] == front_id
        best_piece = jnp.where(hit, got_piece, best_piece)
        best_tags = jnp.where(hit, got_tags, best_tags)
    own_map = best_tags[1:]
    child_blocks = own_map.shape[0]
    block_ranks = jnp.arange(child_blocks, dtype=jnp.int32)

    def locate(first, width):
        target = first + jnp.arange(width, dtype=jnp.int32)
        matches = own_map[:, None] == target[None, :]
        source = jnp.sum(jnp.where(matches, block_ranks[:, None], 0), axis=0)
        return source, jnp.any(matches, axis=0)

    row_src, row_has = locate(row_id * row_blocks, row_blocks)
    col_src, col_has = locate(col_id * col_blocks, col_blocks)
    gathered = lax.all_gather(best_piece, ("row", "col"), axis=0, tiled=False)
    child_tiles = gathered.reshape(row_count, col_count, kid_rows, BS, kid_cols, BS)
    picked = child_tiles[
        (row_src // kid_rows)[:, None],
        (col_src // kid_cols)[None, :],
        (row_src % kid_rows)[:, None],
        :,
        (col_src % kid_cols)[None, :],
        :,
    ]
    keep = row_has[:, None] & col_has[None, :]
    picked = jnp.where(keep[:, :, None, None], picked, 0.0)
    extended = picked.transpose(0, 2, 1, 3).reshape(loc_rows, loc_cols)

    mask_all = block_mask[0].astype(jnp.float32)
    mask_local = lax.dynamic_slice(
        mask_all, (row_id * row_blocks, col_id * col_blocks), (row_blocks, col_blocks)
    )
    assembled = spread(mask_local) * (matrix_in + extended)

    order = pivot[0]
    nblocks = order.shape[0]
    ranks = jnp.arange(nblocks, dtype=jnp.int32)
    position = jnp.sum(jnp.where(order[:, None] == ranks[None, :], ranks[:, None], 0), axis=0)
    alive0 = (position >= 2).astype(jnp.float32)
    alive1 = (position >= 4).astype(jnp.float32)
    piv = [order[k] for k in range(4)]

    def rows_of(blk, mat):
        strip = lax.dynamic_slice_in_dim(mat, (blk % row_blocks) * BS, BS, 0)
        return jnp.where(row_id == blk // row_blocks, strip, 0.0)

    def xor_perm(n, bit):
        return [(i, i ^ bit) for i in range(n)]

    f_rows = jnp.concatenate([rows_of(blk, matrix_in) for blk in piv], axis=0)
    f_rows = f_rows + lax.ppermute(f_rows, "row", xor_perm(row_count, 1))
    half = f_rows.shape[0] // 2
    core = row_id % 2
    mine = jnp.where(core == 0, f_rows[:half], f_rows[half:])
    mine = mine + lax.ppermute(mine, "row", xor_perm(row_count, 2))
    other = lax.ppermute(mine, "row", xor_perm(row_count, 1))
    f_rows = jnp.where(core == 0, jnp.concatenate([mine, other], axis=0), jnp.concatenate([other, mine], axis=0))

    piv_arr = jnp.stack(piv)
    pmatch = own_map[:, None] == piv_arr[None, :]
    prow_src = jnp.sum(jnp.where(pmatch, block_ranks[:, None], 0), axis=0)
    prow_has = jnp.any(pmatch, axis=0)
    picked_rows = child_tiles[
        (prow_src // kid_rows)[:, None],
        (col_src // kid_cols)[None, :],
        (prow_src % kid_rows)[:, None],
        :,
        (col_src % kid_cols)[None, :],
        :,
    ]
    keep_rows = prow_has[:, None] & col_has[None, :]
    picked_rows = jnp.where(keep_rows[:, :, None, None], picked_rows, 0.0)
    placed_rows = picked_rows.transpose(0, 2, 1, 3).reshape(4 * BS, loc_cols)
    mask_piv_rows = lax.dynamic_slice_in_dim(mask_all[piv_arr], col_id * col_blocks, col_blocks, 1)
    row_panels = spread(mask_piv_rows) * (f_rows + placed_rows)

    def cols_of(blk, mat):
        strip = lax.dynamic_slice_in_dim(mat, (blk % col_blocks) * BS, BS, 1)
        return jnp.where(col_id == blk // col_blocks, strip, 0.0)

    corner_x = jnp.concatenate([cols_of(piv[2], row_panels[: 2 * BS]), cols_of(piv[3], row_panels[: 2 * BS])], axis=1)
    corner_y = jnp.concatenate([cols_of(piv[0], row_panels[2 * BS:]), cols_of(piv[1], row_panels[2 * BS:])], axis=1)

    col_parts = [cols_of(blk, assembled) for blk in piv]
    col_payload = jnp.concatenate(
        [jnp.concatenate(col_parts, axis=1), jnp.concatenate([corner_x, corner_y], axis=1)], axis=0
    )
    col_payload = lax.psum(col_payload, "col")
    col_panels = col_payload[:loc_rows]
    corner_x = col_payload[loc_rows:, : 2 * BS]
    corner_y = col_payload[loc_rows:, 2 * BS:]

    alive0_rows = jnp.repeat(lax.dynamic_slice_in_dim(alive0, row_id * row_blocks, row_blocks), BS)
    alive1_rows = jnp.repeat(lax.dynamic_slice_in_dim(alive1, row_id * row_blocks, row_blocks), BS)
    alive0_cb = lax.dynamic_slice_in_dim(alive0, col_id * col_blocks, col_blocks)
    alive1_cb = lax.dynamic_slice_in_dim(alive1, col_id * col_blocks, col_blocks)
    alive0_cols = jnp.repeat(alive0_cb, BS)
    alive1_cols = jnp.repeat(alive1_cb, BS)

    lower0 = dot(col_panels[:, : 2 * BS], diag_inverse[0, 0])
    w0 = lower0 * alive0_rows[:, None]
    mask_rows_p1q1 = lax.dynamic_slice_in_dim(
        jnp.stack([mask_all[:, piv[2]], mask_all[:, piv[3]]], axis=1), row_id * row_blocks, row_blocks, 0
    )
    cp1 = col_panels[:, 2 * BS:] - dot(w0, corner_x) * spread(mask_rows_p1q1)
    lower1 = dot(cp1, diag_inverse[0, 1])
    w1 = lower1 * alive1_rows[:, None]
    rp0 = row_panels[: 2 * BS]
    lower0_p1q1 = dot(corner_y, diag_inverse[0, 0])
    mask_p1q1_cols = lax.dynamic_slice_in_dim(
        jnp.stack([mask_all[piv[2]], mask_all[piv[3]]], axis=0), col_id * col_blocks, col_blocks, 1
    )
    rp1 = row_panels[2 * BS:] - dot(lower0_p1q1, rp0) * spread(mask_p1q1_cols * alive0_cb[None, :])

    lowers = jnp.concatenate([w0, w1], axis=1)
    uppers = jnp.concatenate([rp0 * alive0_cols[None, :], rp1 * alive1_cols[None, :]], axis=0)
    update = dot(lowers, uppers)
    fresh = assembled - update * spread(mask_local)

    replaced = [(piv[0], lower0[:, :BS], alive0_rows), (piv[1], lower0[:, BS:], alive0_rows),
                (piv[2], lower1[:, :BS], alive1_rows), (piv[3], lower1[:, BS:], alive1_rows)]
    for blk, values, live in replaced:
        slot = blk % col_blocks
        current = lax.dynamic_slice_in_dim(fresh, slot * BS, BS, 1)
        written = jnp.where((live[:, None] > 0) & (col_id == blk // col_blocks), values, current)
        fresh = lax.dynamic_update_slice_in_dim(fresh, written, slot * BS, 1)
    return fresh[None]


def solution(mesh):
    placed = (
        P("front", "row", "col"),
        P("front", "row", "col"),
        P("front"),
        P("front", None),
        P("front", None, None),
        P("front", None),
        P("front", None, None, None),
    )
    return jax.shard_map(
        body, mesh=mesh, in_specs=placed, out_specs=P("front", "row", "col"), check_vma=False
    )
```

```python
import jax
import jax.numpy as jnp
from jax import lax
from jax.sharding import PartitionSpec as P

BS = 256


HIGH = lax.Precision.HIGHEST


def dot(a, b):
    return jnp.dot(a, b, precision=HIGH, preferred_element_type=jnp.float32)


def body(front_orig, children, parent_of, child_map, block_mask, pivot, diag_inverse):
    row_count = lax.axis_size("row")
    col_count = lax.axis_size("col")
    front_count = lax.axis_size("front")
    row_id = lax.axis_index("row")
    col_id = lax.axis_index("col")
    front_id = lax.axis_index("front")
    matrix_in = front_orig[0]
    loc_rows, loc_cols = matrix_in.shape
    row_blocks = loc_rows // BS
    col_blocks = loc_cols // BS
    kid_rows = children.shape[1] // BS
    kid_cols = children.shape[2] // BS

    def spread(grid):
        r, c = grid.shape
        return jnp.broadcast_to(grid[:, None, :, None], (r, BS, c, BS)).reshape(r * BS, c * BS)

    piece = children[0]
    tags = jnp.concatenate([parent_of, child_map[0]])
    best_piece = jnp.where(tags[0] == front_id, piece, jnp.zeros_like(piece))
    best_tags = jnp.where(tags[0] == front_id, tags, jnp.zeros_like(tags))
    for shift in range(1, front_count):
        perm = [(i, (i + shift) % front_count) for i in range(front_count)]
        got_piece = lax.ppermute(piece, "front", perm)
        got_tags = lax.ppermute(tags, "front", perm)
        hit = got_tags[0] == front_id
        best_piece = jnp.where(hit, got_piece, best_piece)
        best_tags = jnp.where(hit, got_tags, best_tags)
    own_map = best_tags[1:]
    child_blocks = own_map.shape[0]
    block_ranks = jnp.arange(child_blocks, dtype=jnp.int32)

    def locate(first, width):
        target = first + jnp.arange(width, dtype=jnp.int32)
        matches = own_map[:, None] == target[None, :]
        source = jnp.sum(jnp.where(matches, block_ranks[:, None], 0), axis=0)
        return source, jnp.any(matches, axis=0)

    row_src, row_has = locate(row_id * row_blocks, row_blocks)
    col_src, col_has = locate(col_id * col_blocks, col_blocks)
    gathered = lax.all_gather(best_piece, ("row", "col"), axis=0, tiled=False)
    child_tiles = gathered.reshape(row_count, col_count, kid_rows, BS, kid_cols, BS)
    picked = child_tiles[
        (row_src // kid_rows)[:, None],
        (col_src // kid_cols)[None, :],
        (row_src % kid_rows)[:, None],
        :,
        (col_src % kid_cols)[None, :],
        :,
    ]
    keep = row_has[:, None] & col_has[None, :]
    picked = jnp.where(keep[:, :, None, None], picked, 0.0)
    extended = picked.transpose(0, 2, 1, 3).reshape(loc_rows, loc_cols)

    mask_all = block_mask[0].astype(jnp.float32)
    mask_local = lax.dynamic_slice(
        mask_all, (row_id * row_blocks, col_id * col_blocks), (row_blocks, col_blocks)
    )
    assembled = spread(mask_local) * (matrix_in + extended)

    order = pivot[0]
    nblocks = order.shape[0]
    ranks = jnp.arange(nblocks, dtype=jnp.int32)
    position = jnp.sum(jnp.where(order[:, None] == ranks[None, :], ranks[:, None], 0), axis=0)
    alive0 = (position >= 2).astype(jnp.float32)
    alive1 = (position >= 4).astype(jnp.float32)
    piv = [order[k] for k in range(4)]

    def rows_of(blk, mat):
        strip = lax.dynamic_slice_in_dim(mat, (blk % row_blocks) * BS, BS, 0)
        return jnp.where(row_id == blk // row_blocks, strip, 0.0)

    def xor_perm(n, bit):
        return [(i, i ^ bit) for i in range(n)]

    f_rows = jnp.concatenate([rows_of(blk, matrix_in) for blk in piv], axis=0)
    f_rows = f_rows + lax.ppermute(f_rows, "row", xor_perm(row_count, 1))
    half = f_rows.shape[0] // 2
    core = row_id % 2
    mine = jnp.where(core == 0, f_rows[:half], f_rows[half:])
    mine = mine + lax.ppermute(mine, "row", xor_perm(row_count, 2))
    other = lax.ppermute(mine, "row", xor_perm(row_count, 1))
    f_rows = jnp.where(core == 0, jnp.concatenate([mine, other], axis=0), jnp.concatenate([other, mine], axis=0))

    piv_arr = jnp.stack(piv)
    pmatch = own_map[:, None] == piv_arr[None, :]
    prow_src = jnp.sum(jnp.where(pmatch, block_ranks[:, None], 0), axis=0)
    prow_has = jnp.any(pmatch, axis=0)
    picked_rows = child_tiles[
        (prow_src // kid_rows)[:, None],
        (col_src // kid_cols)[None, :],
        (prow_src % kid_rows)[:, None],
        :,
        (col_src % kid_cols)[None, :],
        :,
    ]
    keep_rows = prow_has[:, None] & col_has[None, :]
    picked_rows = jnp.where(keep_rows[:, :, None, None], picked_rows, 0.0)
    placed_rows = picked_rows.transpose(0, 2, 1, 3).reshape(4 * BS, loc_cols)
    mask_piv_rows = lax.dynamic_slice_in_dim(mask_all[piv_arr], col_id * col_blocks, col_blocks, 1)
    row_panels = spread(mask_piv_rows) * (f_rows + placed_rows)

    def cols_of(blk, mat):
        strip = lax.dynamic_slice_in_dim(mat, (blk % col_blocks) * BS, BS, 1)
        return jnp.where(col_id == blk // col_blocks, strip, 0.0)

    f_x = jnp.concatenate([cols_of(piv[2], f_rows[: 2 * BS]), cols_of(piv[3], f_rows[: 2 * BS])], axis=1)
    f_y = jnp.concatenate([cols_of(piv[0], f_rows[2 * BS:]), cols_of(piv[1], f_rows[2 * BS:])], axis=1)
    col_payload = jnp.concatenate(
        [jnp.concatenate([cols_of(blk, matrix_in) for blk in piv], axis=1), jnp.concatenate([f_x, f_y], axis=1)],
        axis=0,
    )
    col_payload = lax.psum(col_payload, "col")

    def child_blocks_at(rsrc, rhas, csrc, chas):
        got = child_tiles[
            (rsrc // kid_rows)[:, None],
            (csrc // kid_cols)[None, :],
            (rsrc % kid_rows)[:, None],
            :,
            (csrc % kid_cols)[None, :],
            :,
        ]
        got = jnp.where((rhas[:, None] & chas[None, :])[:, :, None, None], got, 0.0)
        nr, nc = got.shape[0], got.shape[1]
        return got.transpose(0, 2, 1, 3).reshape(nr * BS, nc * BS)

    mask_rows_local = lax.dynamic_slice_in_dim(mask_all, row_id * row_blocks, row_blocks, 0)
    col_panels = spread(mask_rows_local[:, piv_arr]) * (
        col_payload[:loc_rows] + child_blocks_at(row_src, row_has, prow_src, prow_has)
    )
    corner_x = spread(mask_all[piv_arr[:2]][:, piv_arr[2:]]) * (
        col_payload[loc_rows:, : 2 * BS] + child_blocks_at(prow_src[:2], prow_has[:2], prow_src[2:], prow_has[2:])
    )
    corner_y = spread(mask_all[piv_arr[2:]][:, piv_arr[:2]]) * (
        col_payload[loc_rows:, 2 * BS:] + child_blocks_at(prow_src[2:], prow_has[2:], prow_src[:2], prow_has[:2])
    )

    alive0_rows = jnp.repeat(lax.dynamic_slice_in_dim(alive0, row_id * row_blocks, row_blocks), BS)
    alive1_rows = jnp.repeat(lax.dynamic_slice_in_dim(alive1, row_id * row_blocks, row_blocks), BS)
    alive0_cb = lax.dynamic_slice_in_dim(alive0, col_id * col_blocks, col_blocks)
    alive1_cb = lax.dynamic_slice_in_dim(alive1, col_id * col_blocks, col_blocks)
    alive0_cols = jnp.repeat(alive0_cb, BS)
    alive1_cols = jnp.repeat(alive1_cb, BS)

    lower0 = dot(col_panels[:, : 2 * BS], diag_inverse[0, 0])
    w0 = lower0 * alive0_rows[:, None]
    mask_rows_p1q1 = lax.dynamic_slice_in_dim(
        jnp.stack([mask_all[:, piv[2]], mask_all[:, piv[3]]], axis=1), row_id * row_blocks, row_blocks, 0
    )
    cp1 = col_panels[:, 2 * BS:] - dot(w0, corner_x) * spread(mask_rows_p1q1)
    lower1 = dot(cp1, diag_inverse[0, 1])
    w1 = lower1 * alive1_rows[:, None]
    rp0 = row_panels[: 2 * BS]
    lower0_p1q1 = dot(corner_y, diag_inverse[0, 0])
    mask_p1q1_cols = lax.dynamic_slice_in_dim(
        jnp.stack([mask_all[piv[2]], mask_all[piv[3]]], axis=0), col_id * col_blocks, col_blocks, 1
    )
    rp1 = row_panels[2 * BS:] - dot(lower0_p1q1, rp0) * spread(mask_p1q1_cols * alive0_cb[None, :])

    lowers = jnp.concatenate([w0, w1], axis=1)
    uppers = jnp.concatenate([rp0 * alive0_cols[None, :], rp1 * alive1_cols[None, :]], axis=0)
    update = dot(lowers, uppers)
    fresh = assembled - update * spread(mask_local)

    replaced = [(piv[0], lower0[:, :BS], alive0_rows), (piv[1], lower0[:, BS:], alive0_rows),
                (piv[2], lower1[:, :BS], alive1_rows), (piv[3], lower1[:, BS:], alive1_rows)]
    for blk, values, live in replaced:
        slot = blk % col_blocks
        current = lax.dynamic_slice_in_dim(fresh, slot * BS, BS, 1)
        written = jnp.where((live[:, None] > 0) & (col_id == blk // col_blocks), values, current)
        fresh = lax.dynamic_update_slice_in_dim(fresh, written, slot * BS, 1)
    return fresh[None]


def solution(mesh):
    placed = (
        P("front", "row", "col"),
        P("front", "row", "col"),
        P("front"),
        P("front", None),
        P("front", None, None),
        P("front", None),
        P("front", None, None, None),
    )
    return jax.shard_map(
        body, mesh=mesh, in_specs=placed, out_specs=P("front", "row", "col"), check_vma=False
    )
```

```python
import jax
import jax.numpy as jnp
from jax import lax
from jax.sharding import PartitionSpec as P

BS = 256


HIGH = lax.Precision.HIGHEST


def dot(a, b):
    return jnp.dot(a, b, precision=HIGH, preferred_element_type=jnp.float32)


def body(front_orig, children, parent_of, child_map, block_mask, pivot, diag_inverse):
    row_count = lax.axis_size("row")
    col_count = lax.axis_size("col")
    front_count = lax.axis_size("front")
    row_id = lax.axis_index("row")
    col_id = lax.axis_index("col")
    front_id = lax.axis_index("front")
    matrix_in = front_orig[0]
    loc_rows, loc_cols = matrix_in.shape
    row_blocks = loc_rows // BS
    col_blocks = loc_cols // BS
    kid_rows = children.shape[1] // BS
    kid_cols = children.shape[2] // BS

    def spread(grid):
        r, c = grid.shape
        return jnp.broadcast_to(grid[:, None, :, None], (r, BS, c, BS)).reshape(r * BS, c * BS)

    piece = children[0]
    tags = jnp.concatenate([parent_of, child_map[0]])
    best_piece = jnp.where(tags[0] == front_id, piece, jnp.zeros_like(piece))
    best_tags = jnp.where(tags[0] == front_id, tags, jnp.zeros_like(tags))
    for shift in range(1, front_count):
        perm = [(i, (i + shift) % front_count) for i in range(front_count)]
        got_piece = lax.ppermute(piece, "front", perm)
        got_tags = lax.ppermute(tags, "front", perm)
        hit = got_tags[0] == front_id
        best_piece = jnp.where(hit, got_piece, best_piece)
        best_tags = jnp.where(hit, got_tags, best_tags)
    own_map = best_tags[1:]
    child_blocks = own_map.shape[0]
    block_ranks = jnp.arange(child_blocks, dtype=jnp.int32)

    def locate(first, width):
        target = first + jnp.arange(width, dtype=jnp.int32)
        matches = own_map[:, None] == target[None, :]
        source = jnp.sum(jnp.where(matches, block_ranks[:, None], 0), axis=0)
        return source, jnp.any(matches, axis=0)

    row_src, row_has = locate(row_id * row_blocks, row_blocks)
    col_src, col_has = locate(col_id * col_blocks, col_blocks)
    gathered = lax.all_gather(best_piece, ("row", "col"), axis=0, tiled=False)
    child4 = (
        gathered.reshape(row_count, col_count, kid_rows, BS, kid_cols, BS)
        .transpose(0, 2, 3, 1, 4, 5)
        .reshape(row_count * kid_rows, BS, col_count * kid_cols, BS)
    )

    def child_blocks_at(rsrc, rhas, csrc, chas):
        got = jnp.take(child4, rsrc, axis=0, mode="clip")
        got = jnp.take(got, csrc, axis=2, mode="clip")
        keep = rhas[:, None, None, None] & chas[None, None, :, None]
        got = jnp.where(keep, got, 0.0)
        return got.reshape(got.shape[0] * BS, got.shape[2] * BS)

    extended = child_blocks_at(row_src, row_has, col_src, col_has)

    mask_all = block_mask[0].astype(jnp.float32)
    mask_local = lax.dynamic_slice(
        mask_all, (row_id * row_blocks, col_id * col_blocks), (row_blocks, col_blocks)
    )
    assembled = spread(mask_local) * (matrix_in + extended)

    order = pivot[0]
    nblocks = order.shape[0]
    ranks = jnp.arange(nblocks, dtype=jnp.int32)
    position = jnp.sum(jnp.where(order[:, None] == ranks[None, :], ranks[:, None], 0), axis=0)
    alive0 = (position >= 2).astype(jnp.float32)
    alive1 = (position >= 4).astype(jnp.float32)
    piv = [order[k] for k in range(4)]

    def rows_of(blk, mat):
        strip = lax.dynamic_slice_in_dim(mat, (blk % row_blocks) * BS, BS, 0)
        return jnp.where(row_id == blk // row_blocks, strip, 0.0)

    def xor_perm(n, bit):
        return [(i, i ^ bit) for i in range(n)]

    f_rows = jnp.concatenate([rows_of(blk, matrix_in) for blk in piv], axis=0)
    f_rows = f_rows + lax.ppermute(f_rows, "row", xor_perm(row_count, 1))
    half = f_rows.shape[0] // 2
    core = row_id % 2
    mine = jnp.where(core == 0, f_rows[:half], f_rows[half:])
    mine = mine + lax.ppermute(mine, "row", xor_perm(row_count, 2))
    other = lax.ppermute(mine, "row", xor_perm(row_count, 1))
    f_rows = jnp.where(core == 0, jnp.concatenate([mine, other], axis=0), jnp.concatenate([other, mine], axis=0))

    piv_arr = jnp.stack(piv)
    pmatch = own_map[:, None] == piv_arr[None, :]
    prow_src = jnp.sum(jnp.where(pmatch, block_ranks[:, None], 0), axis=0)
    prow_has = jnp.any(pmatch, axis=0)
    placed_rows = child_blocks_at(prow_src, prow_has, col_src, col_has)
    mask_piv_rows = lax.dynamic_slice_in_dim(mask_all[piv_arr], col_id * col_blocks, col_blocks, 1)
    row_panels = spread(mask_piv_rows) * (f_rows + placed_rows)

    def cols_of(blk, mat):
        strip = lax.dynamic_slice_in_dim(mat, (blk % col_blocks) * BS, BS, 1)
        return jnp.where(col_id == blk // col_blocks, strip, 0.0)

    f_x = jnp.concatenate([cols_of(piv[2], f_rows[: 2 * BS]), cols_of(piv[3], f_rows[: 2 * BS])], axis=1)
    f_y = jnp.concatenate([cols_of(piv[0], f_rows[2 * BS:]), cols_of(piv[1], f_rows[2 * BS:])], axis=1)
    col_payload = jnp.concatenate(
        [jnp.concatenate([cols_of(blk, matrix_in) for blk in piv], axis=1), jnp.concatenate([f_x, f_y], axis=1)],
        axis=0,
    )
    col_payload = lax.psum(col_payload, "col")

    mask_rows_local = lax.dynamic_slice_in_dim(mask_all, row_id * row_blocks, row_blocks, 0)
    col_panels = spread(mask_rows_local[:, piv_arr]) * (
        col_payload[:loc_rows] + child_blocks_at(row_src, row_has, prow_src, prow_has)
    )
    corner_x = spread(mask_all[piv_arr[:2]][:, piv_arr[2:]]) * (
        col_payload[loc_rows:, : 2 * BS] + child_blocks_at(prow_src[:2], prow_has[:2], prow_src[2:], prow_has[2:])
    )
    corner_y = spread(mask_all[piv_arr[2:]][:, piv_arr[:2]]) * (
        col_payload[loc_rows:, 2 * BS:] + child_blocks_at(prow_src[2:], prow_has[2:], prow_src[:2], prow_has[:2])
    )

    alive0_rows = jnp.repeat(lax.dynamic_slice_in_dim(alive0, row_id * row_blocks, row_blocks), BS)
    alive1_rows = jnp.repeat(lax.dynamic_slice_in_dim(alive1, row_id * row_blocks, row_blocks), BS)
    alive0_cb = lax.dynamic_slice_in_dim(alive0, col_id * col_blocks, col_blocks)
    alive1_cb = lax.dynamic_slice_in_dim(alive1, col_id * col_blocks, col_blocks)
    alive0_cols = jnp.repeat(alive0_cb, BS)
    alive1_cols = jnp.repeat(alive1_cb, BS)

    lower0 = dot(col_panels[:, : 2 * BS], diag_inverse[0, 0])
    w0 = lower0 * alive0_rows[:, None]
    mask_rows_p1q1 = lax.dynamic_slice_in_dim(
        jnp.stack([mask_all[:, piv[2]], mask_all[:, piv[3]]], axis=1), row_id * row_blocks, row_blocks, 0
    )
    cp1 = col_panels[:, 2 * BS:] - dot(w0, corner_x) * spread(mask_rows_p1q1)
    lower1 = dot(cp1, diag_inverse[0, 1])
    w1 = lower1 * alive1_rows[:, None]
    rp0 = row_panels[: 2 * BS]
    lower0_p1q1 = dot(corner_y, diag_inverse[0, 0])
    mask_p1q1_cols = lax.dynamic_slice_in_dim(
        jnp.stack([mask_all[piv[2]], mask_all[piv[3]]], axis=0), col_id * col_blocks, col_blocks, 1
    )
    rp1 = row_panels[2 * BS:] - dot(lower0_p1q1, rp0) * spread(mask_p1q1_cols * alive0_cb[None, :])

    lowers = jnp.concatenate([w0, w1], axis=1)
    uppers = jnp.concatenate([rp0 * alive0_cols[None, :], rp1 * alive1_cols[None, :]], axis=0)
    update = dot(lowers, uppers)
    fresh = assembled - update * spread(mask_local)

    lower_blocks = jnp.stack([lower0[:, :BS], lower0[:, BS:], lower1[:, :BS], lower1[:, BS:]])
    live_blocks = jnp.stack([alive0_rows, alive0_rows, alive1_rows, alive1_rows]) > 0
    local_blk = col_id * col_blocks + jnp.arange(col_blocks, dtype=jnp.int32)
    hits = piv_arr[None, :] == local_blk[:, None]
    which = jnp.sum(jnp.where(hits, jnp.arange(4, dtype=jnp.int32)[None, :], 0), axis=1)
    owned = jnp.any(hits, axis=1)
    take_lower = jnp.concatenate(
        [jnp.broadcast_to((live_blocks[which[j]] & owned[j])[:, None], (loc_rows, BS)) for j in range(col_blocks)],
        axis=1,
    )
    lower_cols = jnp.concatenate([lower_blocks[which[j]] for j in range(col_blocks)], axis=1)
    fresh = jnp.where(take_lower, lower_cols, fresh)
    return fresh[None]


def solution(mesh):
    placed = (
        P("front", "row", "col"),
        P("front", "row", "col"),
        P("front"),
        P("front", None),
        P("front", None, None),
        P("front", None),
        P("front", None, None, None),
    )
    return jax.shard_map(
        body, mesh=mesh, in_specs=placed, out_specs=P("front", "row", "col"), check_vma=False
    )
```

```python
import jax
import jax.numpy as jnp
from jax import lax
from jax.sharding import PartitionSpec as P

BS = 256


HIGH = lax.Precision.HIGHEST


def dot(a, b):
    return jnp.dot(a, b, precision=HIGH, preferred_element_type=jnp.float32)


def body(front_orig, children, parent_of, child_map, block_mask, pivot, diag_inverse):
    row_count = lax.axis_size("row")
    col_count = lax.axis_size("col")
    front_count = lax.axis_size("front")
    row_id = lax.axis_index("row")
    col_id = lax.axis_index("col")
    front_id = lax.axis_index("front")
    matrix_in = front_orig[0]
    loc_rows, loc_cols = matrix_in.shape
    row_blocks = loc_rows // BS
    col_blocks = loc_cols // BS
    kid_rows = children.shape[1] // BS
    kid_cols = children.shape[2] // BS

    def spread(grid):
        r, c = grid.shape
        return jnp.broadcast_to(grid[:, None, :, None], (r, BS, c, BS)).reshape(r * BS, c * BS)

    piece = children[0]
    tags = jnp.concatenate([parent_of, child_map[0]])
    best_piece = jnp.where(tags[0] == front_id, piece, jnp.zeros_like(piece))
    best_tags = jnp.where(tags[0] == front_id, tags, jnp.zeros_like(tags))
    for shift in range(1, front_count):
        perm = [(i, (i + shift) % front_count) for i in range(front_count)]
        got_piece = lax.ppermute(piece, "front", perm)
        got_tags = lax.ppermute(tags, "front", perm)
        hit = got_tags[0] == front_id
        best_piece = jnp.where(hit, got_piece, best_piece)
        best_tags = jnp.where(hit, got_tags, best_tags)
    own_map = best_tags[1:]
    child_blocks = own_map.shape[0]
    block_ranks = jnp.arange(child_blocks, dtype=jnp.int32)

    def locate(first, width):
        target = first + jnp.arange(width, dtype=jnp.int32)
        matches = own_map[:, None] == target[None, :]
        source = jnp.sum(jnp.where(matches, block_ranks[:, None], 0), axis=0)
        return source, jnp.any(matches, axis=0)

    row_src, row_has = locate(row_id * row_blocks, row_blocks)
    col_src, col_has = locate(col_id * col_blocks, col_blocks)
    gathered = lax.all_gather(best_piece, ("row", "col"), axis=0, tiled=False)
    def child_block(blk_r, blk_c):
        start = ((blk_r // kid_rows) * col_count + blk_c // kid_cols, (blk_r % kid_rows) * BS, (blk_c % kid_cols) * BS)
        return lax.dynamic_slice(gathered, start, (1, BS, BS))[0]

    def child_blocks_at(rsrc, rhas, csrc, chas):
        rows = []
        for i in range(rsrc.shape[0]):
            row = [jnp.where(rhas[i] & chas[j], child_block(rsrc[i], csrc[j]), 0.0) for j in range(csrc.shape[0])]
            rows.append(jnp.concatenate(row, axis=1))
        return jnp.concatenate(rows, axis=0)

    extended = child_blocks_at(row_src, row_has, col_src, col_has)

    mask_all = block_mask[0].astype(jnp.float32)
    mask_local = lax.dynamic_slice(
        mask_all, (row_id * row_blocks, col_id * col_blocks), (row_blocks, col_blocks)
    )
    assembled = spread(mask_local) * (matrix_in + extended)

    order = pivot[0]
    nblocks = order.shape[0]
    ranks = jnp.arange(nblocks, dtype=jnp.int32)
    position = jnp.sum(jnp.where(order[:, None] == ranks[None, :], ranks[:, None], 0), axis=0)
    alive0 = (position >= 2).astype(jnp.float32)
    alive1 = (position >= 4).astype(jnp.float32)
    piv = [order[k] for k in range(4)]

    def rows_of(blk, mat):
        strip = lax.dynamic_slice_in_dim(mat, (blk % row_blocks) * BS, BS, 0)
        return jnp.where(row_id == blk // row_blocks, strip, 0.0)

    def xor_perm(n, bit):
        return [(i, i ^ bit) for i in range(n)]

    f_rows = jnp.concatenate([rows_of(blk, matrix_in) for blk in piv], axis=0)
    f_rows = f_rows + lax.ppermute(f_rows, "row", xor_perm(row_count, 1))
    half = f_rows.shape[0] // 2
    core = row_id % 2
    mine = jnp.where(core == 0, f_rows[:half], f_rows[half:])
    mine = mine + lax.ppermute(mine, "row", xor_perm(row_count, 2))
    other = lax.ppermute(mine, "row", xor_perm(row_count, 1))
    f_rows = jnp.where(core == 0, jnp.concatenate([mine, other], axis=0), jnp.concatenate([other, mine], axis=0))

    piv_arr = jnp.stack(piv)
    pmatch = own_map[:, None] == piv_arr[None, :]
    prow_src = jnp.sum(jnp.where(pmatch, block_ranks[:, None], 0), axis=0)
    prow_has = jnp.any(pmatch, axis=0)
    placed_rows = child_blocks_at(prow_src, prow_has, col_src, col_has)
    mask_piv_rows = lax.dynamic_slice_in_dim(mask_all[piv_arr], col_id * col_blocks, col_blocks, 1)
    row_panels = spread(mask_piv_rows) * (f_rows + placed_rows)

    def cols_of(blk, mat):
        strip = lax.dynamic_slice_in_dim(mat, (blk % col_blocks) * BS, BS, 1)
        return jnp.where(col_id == blk // col_blocks, strip, 0.0)

    f_x = jnp.concatenate([cols_of(piv[2], f_rows[: 2 * BS]), cols_of(piv[3], f_rows[: 2 * BS])], axis=1)
    f_y = jnp.concatenate([cols_of(piv[0], f_rows[2 * BS:]), cols_of(piv[1], f_rows[2 * BS:])], axis=1)
    col_payload = jnp.concatenate(
        [jnp.concatenate([cols_of(blk, matrix_in) for blk in piv], axis=1), jnp.concatenate([f_x, f_y], axis=1)],
        axis=0,
    )
    col_payload = lax.psum(col_payload, "col")

    mask_rows_local = lax.dynamic_slice_in_dim(mask_all, row_id * row_blocks, row_blocks, 0)
    col_panels = spread(mask_rows_local[:, piv_arr]) * (
        col_payload[:loc_rows] + child_blocks_at(row_src, row_has, prow_src, prow_has)
    )
    corner_x = spread(mask_all[piv_arr[:2]][:, piv_arr[2:]]) * (
        col_payload[loc_rows:, : 2 * BS] + child_blocks_at(prow_src[:2], prow_has[:2], prow_src[2:], prow_has[2:])
    )
    corner_y = spread(mask_all[piv_arr[2:]][:, piv_arr[:2]]) * (
        col_payload[loc_rows:, 2 * BS:] + child_blocks_at(prow_src[2:], prow_has[2:], prow_src[:2], prow_has[:2])
    )

    alive0_rows = jnp.repeat(lax.dynamic_slice_in_dim(alive0, row_id * row_blocks, row_blocks), BS)
    alive1_rows = jnp.repeat(lax.dynamic_slice_in_dim(alive1, row_id * row_blocks, row_blocks), BS)
    alive0_cb = lax.dynamic_slice_in_dim(alive0, col_id * col_blocks, col_blocks)
    alive1_cb = lax.dynamic_slice_in_dim(alive1, col_id * col_blocks, col_blocks)
    alive0_cols = jnp.repeat(alive0_cb, BS)
    alive1_cols = jnp.repeat(alive1_cb, BS)

    lower0 = dot(col_panels[:, : 2 * BS], diag_inverse[0, 0])
    w0 = lower0 * alive0_rows[:, None]
    mask_rows_p1q1 = lax.dynamic_slice_in_dim(
        jnp.stack([mask_all[:, piv[2]], mask_all[:, piv[3]]], axis=1), row_id * row_blocks, row_blocks, 0
    )
    cp1 = col_panels[:, 2 * BS:] - dot(w0, corner_x) * spread(mask_rows_p1q1)
    lower1 = dot(cp1, diag_inverse[0, 1])
    w1 = lower1 * alive1_rows[:, None]
    rp0 = row_panels[: 2 * BS]
    lower0_p1q1 = dot(corner_y, diag_inverse[0, 0])
    mask_p1q1_cols = lax.dynamic_slice_in_dim(
        jnp.stack([mask_all[piv[2]], mask_all[piv[3]]], axis=0), col_id * col_blocks, col_blocks, 1
    )
    rp1 = row_panels[2 * BS:] - dot(lower0_p1q1, rp0) * spread(mask_p1q1_cols * alive0_cb[None, :])

    lowers = jnp.concatenate([w0, w1], axis=1)
    uppers = jnp.concatenate([rp0 * alive0_cols[None, :], rp1 * alive1_cols[None, :]], axis=0)
    update = dot(lowers, uppers)
    fresh = assembled - update * spread(mask_local)

    lower_blocks = jnp.stack([lower0[:, :BS], lower0[:, BS:], lower1[:, :BS], lower1[:, BS:]])
    live_blocks = jnp.stack([alive0_rows, alive0_rows, alive1_rows, alive1_rows]) > 0
    local_blk = col_id * col_blocks + jnp.arange(col_blocks, dtype=jnp.int32)
    hits = piv_arr[None, :] == local_blk[:, None]
    which = jnp.sum(jnp.where(hits, jnp.arange(4, dtype=jnp.int32)[None, :], 0), axis=1)
    owned = jnp.any(hits, axis=1)
    take_lower = jnp.concatenate(
        [jnp.broadcast_to((live_blocks[which[j]] & owned[j])[:, None], (loc_rows, BS)) for j in range(col_blocks)],
        axis=1,
    )
    lower_cols = jnp.concatenate([lower_blocks[which[j]] for j in range(col_blocks)], axis=1)
    fresh = jnp.where(take_lower, lower_cols, fresh)
    return fresh[None]


def solution(mesh):
    placed = (
        P("front", "row", "col"),
        P("front", "row", "col"),
        P("front"),
        P("front", None),
        P("front", None, None),
        P("front", None),
        P("front", None, None, None),
    )
    return jax.shard_map(
        body, mesh=mesh, in_specs=placed, out_specs=P("front", "row", "col"), check_vma=False
    )
```

```python
import jax
import jax.numpy as jnp
from jax import lax
from jax.sharding import PartitionSpec as P

BS = 256


HIGH = lax.Precision.HIGH


def dot(a, b):
    return jnp.dot(a, b, precision=HIGH, preferred_element_type=jnp.float32)


def body(front_orig, children, parent_of, child_map, block_mask, pivot, diag_inverse):
    row_count = lax.axis_size("row")
    col_count = lax.axis_size("col")
    front_count = lax.axis_size("front")
    row_id = lax.axis_index("row")
    col_id = lax.axis_index("col")
    front_id = lax.axis_index("front")
    matrix_in = front_orig[0]
    loc_rows, loc_cols = matrix_in.shape
    row_blocks = loc_rows // BS
    col_blocks = loc_cols // BS
    kid_rows = children.shape[1] // BS
    kid_cols = children.shape[2] // BS

    def spread(grid):
        r, c = grid.shape
        return jnp.broadcast_to(grid[:, None, :, None], (r, BS, c, BS)).reshape(r * BS, c * BS)

    piece = children[0]
    tags = jnp.concatenate([parent_of, child_map[0]])
    best_piece = jnp.where(tags[0] == front_id, piece, jnp.zeros_like(piece))
    best_tags = jnp.where(tags[0] == front_id, tags, jnp.zeros_like(tags))
    for shift in range(1, front_count):
        perm = [(i, (i + shift) % front_count) for i in range(front_count)]
        got_piece = lax.ppermute(piece, "front", perm)
        got_tags = lax.ppermute(tags, "front", perm)
        hit = got_tags[0] == front_id
        best_piece = jnp.where(hit, got_piece, best_piece)
        best_tags = jnp.where(hit, got_tags, best_tags)
    own_map = best_tags[1:]
    child_blocks = own_map.shape[0]
    block_ranks = jnp.arange(child_blocks, dtype=jnp.int32)

    def locate(first, width):
        target = first + jnp.arange(width, dtype=jnp.int32)
        matches = own_map[:, None] == target[None, :]
        source = jnp.sum(jnp.where(matches, block_ranks[:, None], 0), axis=0)
        return source, jnp.any(matches, axis=0)

    row_src, row_has = locate(row_id * row_blocks, row_blocks)
    col_src, col_has = locate(col_id * col_blocks, col_blocks)
    gathered = lax.all_gather(best_piece, ("row", "col"), axis=0, tiled=False)
    child_tiles = gathered.reshape(row_count, col_count, kid_rows, BS, kid_cols, BS)
    picked = child_tiles[
        (row_src // kid_rows)[:, None],
        (col_src // kid_cols)[None, :],
        (row_src % kid_rows)[:, None],
        :,
        (col_src % kid_cols)[None, :],
        :,
    ]
    keep = row_has[:, None] & col_has[None, :]
    picked = jnp.where(keep[:, :, None, None], picked, 0.0)
    extended = picked.transpose(0, 2, 1, 3).reshape(loc_rows, loc_cols)

    mask_all = block_mask[0].astype(jnp.float32)
    mask_local = lax.dynamic_slice(
        mask_all, (row_id * row_blocks, col_id * col_blocks), (row_blocks, col_blocks)
    )
    assembled = spread(mask_local) * (matrix_in + extended)

    order = pivot[0]
    nblocks = order.shape[0]
    ranks = jnp.arange(nblocks, dtype=jnp.int32)
    position = jnp.sum(jnp.where(order[:, None] == ranks[None, :], ranks[:, None], 0), axis=0)
    alive0 = (position >= 2).astype(jnp.float32)
    alive1 = (position >= 4).astype(jnp.float32)
    piv = [order[k] for k in range(4)]

    def rows_of(blk, mat):
        strip = lax.dynamic_slice_in_dim(mat, (blk % row_blocks) * BS, BS, 0)
        return jnp.where(row_id == blk // row_blocks, strip, 0.0)

    def xor_perm(n, bit):
        return [(i, i ^ bit) for i in range(n)]

    f_rows = jnp.concatenate([rows_of(blk, matrix_in) for blk in piv], axis=0)
    f_rows = f_rows + lax.ppermute(f_rows, "row", xor_perm(row_count, 1))
    half = f_rows.shape[0] // 2
    core = row_id % 2
    mine = jnp.where(core == 0, f_rows[:half], f_rows[half:])
    mine = mine + lax.ppermute(mine, "row", xor_perm(row_count, 2))
    other = lax.ppermute(mine, "row", xor_perm(row_count, 1))
    f_rows = jnp.where(core == 0, jnp.concatenate([mine, other], axis=0), jnp.concatenate([other, mine], axis=0))

    piv_arr = jnp.stack(piv)
    pmatch = own_map[:, None] == piv_arr[None, :]
    prow_src = jnp.sum(jnp.where(pmatch, block_ranks[:, None], 0), axis=0)
    prow_has = jnp.any(pmatch, axis=0)
    picked_rows = child_tiles[
        (prow_src // kid_rows)[:, None],
        (col_src // kid_cols)[None, :],
        (prow_src % kid_rows)[:, None],
        :,
        (col_src % kid_cols)[None, :],
        :,
    ]
    keep_rows = prow_has[:, None] & col_has[None, :]
    picked_rows = jnp.where(keep_rows[:, :, None, None], picked_rows, 0.0)
    placed_rows = picked_rows.transpose(0, 2, 1, 3).reshape(4 * BS, loc_cols)
    mask_piv_rows = lax.dynamic_slice_in_dim(mask_all[piv_arr], col_id * col_blocks, col_blocks, 1)
    row_panels = spread(mask_piv_rows) * (f_rows + placed_rows)

    def cols_of(blk, mat):
        strip = lax.dynamic_slice_in_dim(mat, (blk % col_blocks) * BS, BS, 1)
        return jnp.where(col_id == blk // col_blocks, strip, 0.0)

    f_x = jnp.concatenate([cols_of(piv[2], f_rows[: 2 * BS]), cols_of(piv[3], f_rows[: 2 * BS])], axis=1)
    f_y = jnp.concatenate([cols_of(piv[0], f_rows[2 * BS:]), cols_of(piv[1], f_rows[2 * BS:])], axis=1)
    col_payload = jnp.concatenate(
        [jnp.concatenate([cols_of(blk, matrix_in) for blk in piv], axis=1), jnp.concatenate([f_x, f_y], axis=1)],
        axis=0,
    )
    col_payload = lax.psum(col_payload, "col")

    def child_blocks_at(rsrc, rhas, csrc, chas):
        got = child_tiles[
            (rsrc // kid_rows)[:, None],
            (csrc // kid_cols)[None, :],
            (rsrc % kid_rows)[:, None],
            :,
            (csrc % kid_cols)[None, :],
            :,
        ]
        got = jnp.where((rhas[:, None] & chas[None, :])[:, :, None, None], got, 0.0)
        nr, nc = got.shape[0], got.shape[1]
        return got.transpose(0, 2, 1, 3).reshape(nr * BS, nc * BS)

    mask_rows_local = lax.dynamic_slice_in_dim(mask_all, row_id * row_blocks, row_blocks, 0)
    col_panels = spread(mask_rows_local[:, piv_arr]) * (
        col_payload[:loc_rows] + child_blocks_at(row_src, row_has, prow_src, prow_has)
    )
    corner_x = spread(mask_all[piv_arr[:2]][:, piv_arr[2:]]) * (
        col_payload[loc_rows:, : 2 * BS] + child_blocks_at(prow_src[:2], prow_has[:2], prow_src[2:], prow_has[2:])
    )
    corner_y = spread(mask_all[piv_arr[2:]][:, piv_arr[:2]]) * (
        col_payload[loc_rows:, 2 * BS:] + child_blocks_at(prow_src[2:], prow_has[2:], prow_src[:2], prow_has[:2])
    )

    alive0_rows = jnp.repeat(lax.dynamic_slice_in_dim(alive0, row_id * row_blocks, row_blocks), BS)
    alive1_rows = jnp.repeat(lax.dynamic_slice_in_dim(alive1, row_id * row_blocks, row_blocks), BS)
    alive0_cb = lax.dynamic_slice_in_dim(alive0, col_id * col_blocks, col_blocks)
    alive1_cb = lax.dynamic_slice_in_dim(alive1, col_id * col_blocks, col_blocks)
    alive0_cols = jnp.repeat(alive0_cb, BS)
    alive1_cols = jnp.repeat(alive1_cb, BS)

    lower0 = dot(col_panels[:, : 2 * BS], diag_inverse[0, 0])
    w0 = lower0 * alive0_rows[:, None]
    mask_rows_p1q1 = lax.dynamic_slice_in_dim(
        jnp.stack([mask_all[:, piv[2]], mask_all[:, piv[3]]], axis=1), row_id * row_blocks, row_blocks, 0
    )
    cp1 = col_panels[:, 2 * BS:] - dot(w0, corner_x) * spread(mask_rows_p1q1)
    lower1 = dot(cp1, diag_inverse[0, 1])
    w1 = lower1 * alive1_rows[:, None]
    rp0 = row_panels[: 2 * BS]
    lower0_p1q1 = dot(corner_y, diag_inverse[0, 0])
    mask_p1q1_cols = lax.dynamic_slice_in_dim(
        jnp.stack([mask_all[piv[2]], mask_all[piv[3]]], axis=0), col_id * col_blocks, col_blocks, 1
    )
    rp1 = row_panels[2 * BS:] - dot(lower0_p1q1, rp0) * spread(mask_p1q1_cols * alive0_cb[None, :])

    lowers = jnp.concatenate([w0, w1], axis=1)
    uppers = jnp.concatenate([rp0 * alive0_cols[None, :], rp1 * alive1_cols[None, :]], axis=0)
    update = dot(lowers, uppers)
    fresh = assembled - update * spread(mask_local)

    replaced = [(piv[0], lower0[:, :BS], alive0_rows), (piv[1], lower0[:, BS:], alive0_rows),
                (piv[2], lower1[:, :BS], alive1_rows), (piv[3], lower1[:, BS:], alive1_rows)]
    for blk, values, live in replaced:
        slot = blk % col_blocks
        current = lax.dynamic_slice_in_dim(fresh, slot * BS, BS, 1)
        written = jnp.where((live[:, None] > 0) & (col_id == blk // col_blocks), values, current)
        fresh = lax.dynamic_update_slice_in_dim(fresh, written, slot * BS, 1)
    return fresh[None]


def solution(mesh):
    placed = (
        P("front", "row", "col"),
        P("front", "row", "col"),
        P("front"),
        P("front", None),
        P("front", None, None),
        P("front", None),
        P("front", None, None, None),
    )
    return jax.shard_map(
        body, mesh=mesh, in_specs=placed, out_specs=P("front", "row", "col"), check_vma=False
    )
```

```python
import jax
import jax.numpy as jnp
from jax import lax
from jax.sharding import PartitionSpec as P

BS = 256


HIGH = lax.Precision.HIGH


def dot(a, b):
    return jnp.dot(a, b, precision=HIGH, preferred_element_type=jnp.float32)


def body(front_orig, children, parent_of, child_map, block_mask, pivot, diag_inverse):
    row_count = lax.axis_size("row")
    col_count = lax.axis_size("col")
    front_count = lax.axis_size("front")
    row_id = lax.axis_index("row")
    col_id = lax.axis_index("col")
    front_id = lax.axis_index("front")
    matrix_in = front_orig[0]
    loc_rows, loc_cols = matrix_in.shape
    row_blocks = loc_rows // BS
    col_blocks = loc_cols // BS
    kid_rows = children.shape[1] // BS
    kid_cols = children.shape[2] // BS

    def spread(grid):
        r, c = grid.shape
        return jnp.broadcast_to(grid[:, None, :, None], (r, BS, c, BS)).reshape(r * BS, c * BS)

    piece = children[0]
    tags = jnp.concatenate([parent_of, child_map[0]])
    best_piece = jnp.where(tags[0] == front_id, piece, jnp.zeros_like(piece))
    best_tags = jnp.where(tags[0] == front_id, tags, jnp.zeros_like(tags))
    for shift in range(1, front_count):
        perm = [(i, (i + shift) % front_count) for i in range(front_count)]
        got_piece = lax.ppermute(piece, "front", perm)
        got_tags = lax.ppermute(tags, "front", perm)
        hit = got_tags[0] == front_id
        best_piece = jnp.where(hit, got_piece, best_piece)
        best_tags = jnp.where(hit, got_tags, best_tags)
    own_map = best_tags[1:]
    child_blocks = own_map.shape[0]
    block_ranks = jnp.arange(child_blocks, dtype=jnp.int32)

    def locate(first, width):
        target = first + jnp.arange(width, dtype=jnp.int32)
        matches = own_map[:, None] == target[None, :]
        source = jnp.sum(jnp.where(matches, block_ranks[:, None], 0), axis=0)
        return source, jnp.any(matches, axis=0)

    row_src, row_has = locate(row_id * row_blocks, row_blocks)
    col_src, col_has = locate(col_id * col_blocks, col_blocks)
    gathered = lax.all_gather(best_piece, ("row", "col"), axis=0, tiled=False)
    child_tiles = gathered.reshape(row_count, col_count, kid_rows, BS, kid_cols, BS)
    picked = child_tiles[
        (row_src // kid_rows)[:, None],
        (col_src // kid_cols)[None, :],
        (row_src % kid_rows)[:, None],
        :,
        (col_src % kid_cols)[None, :],
        :,
    ]
    keep = row_has[:, None] & col_has[None, :]
    picked = jnp.where(keep[:, :, None, None], picked, 0.0)
    extended = picked.transpose(0, 2, 1, 3).reshape(loc_rows, loc_cols)

    mask_all = block_mask[0].astype(jnp.float32)
    mask_local = lax.dynamic_slice(
        mask_all, (row_id * row_blocks, col_id * col_blocks), (row_blocks, col_blocks)
    )
    assembled = spread(mask_local) * (matrix_in + extended)

    order = pivot[0]
    nblocks = order.shape[0]
    ranks = jnp.arange(nblocks, dtype=jnp.int32)
    position = jnp.sum(jnp.where(order[:, None] == ranks[None, :], ranks[:, None], 0), axis=0)
    alive0 = (position >= 2).astype(jnp.float32)
    alive1 = (position >= 4).astype(jnp.float32)
    piv = [order[k] for k in range(4)]

    def rows_of(blk, mat):
        strip = lax.dynamic_slice_in_dim(mat, (blk % row_blocks) * BS, BS, 0)
        return jnp.where(row_id == blk // row_blocks, strip, 0.0)

    def xor_perm(n, bit):
        return [(i, i ^ bit) for i in range(n)]

    f_rows = jnp.concatenate([rows_of(blk, matrix_in) for blk in piv], axis=0)
    f_rows = f_rows + lax.ppermute(f_rows, "row", xor_perm(row_count, 1))
    half = f_rows.shape[0] // 2
    core = row_id % 2
    mine = jnp.where(core == 0, f_rows[:half], f_rows[half:])
    mine = mine + lax.ppermute(mine, "row", xor_perm(row_count, 2))
    other = lax.ppermute(mine, "row", xor_perm(row_count, 1))
    f_rows = jnp.where(core == 0, jnp.concatenate([mine, other], axis=0), jnp.concatenate([other, mine], axis=0))

    piv_arr = jnp.stack(piv)
    pmatch = own_map[:, None] == piv_arr[None, :]
    prow_src = jnp.sum(jnp.where(pmatch, block_ranks[:, None], 0), axis=0)
    prow_has = jnp.any(pmatch, axis=0)
    picked_rows = child_tiles[
        (prow_src // kid_rows)[:, None],
        (col_src // kid_cols)[None, :],
        (prow_src % kid_rows)[:, None],
        :,
        (col_src % kid_cols)[None, :],
        :,
    ]
    keep_rows = prow_has[:, None] & col_has[None, :]
    picked_rows = jnp.where(keep_rows[:, :, None, None], picked_rows, 0.0)
    placed_rows = picked_rows.transpose(0, 2, 1, 3).reshape(4 * BS, loc_cols)
    mask_piv_rows = lax.dynamic_slice_in_dim(mask_all[piv_arr], col_id * col_blocks, col_blocks, 1)
    row_panels = spread(mask_piv_rows) * (f_rows + placed_rows)

    def cols_of(blk, mat):
        strip = lax.dynamic_slice_in_dim(mat, (blk % col_blocks) * BS, BS, 1)
        return jnp.where(col_id == blk // col_blocks, strip, 0.0)

    f_x = jnp.concatenate([cols_of(piv[2], f_rows[: 2 * BS]), cols_of(piv[3], f_rows[: 2 * BS])], axis=1)
    f_y = jnp.concatenate([cols_of(piv[0], f_rows[2 * BS:]), cols_of(piv[1], f_rows[2 * BS:])], axis=1)
    col_payload = jnp.concatenate(
        [jnp.concatenate([cols_of(blk, matrix_in) for blk in piv], axis=1), jnp.concatenate([f_x, f_y], axis=1)],
        axis=0,
    )
    col_payload = lax.psum(col_payload, "col")

    def child_blocks_at(rsrc, rhas, csrc, chas):
        got = child_tiles[
            (rsrc // kid_rows)[:, None],
            (csrc // kid_cols)[None, :],
            (rsrc % kid_rows)[:, None],
            :,
            (csrc % kid_cols)[None, :],
            :,
        ]
        got = jnp.where((rhas[:, None] & chas[None, :])[:, :, None, None], got, 0.0)
        nr, nc = got.shape[0], got.shape[1]
        return got.transpose(0, 2, 1, 3).reshape(nr * BS, nc * BS)

    mask_rows_local = lax.dynamic_slice_in_dim(mask_all, row_id * row_blocks, row_blocks, 0)
    col_panels = spread(mask_rows_local[:, piv_arr]) * (
        col_payload[:loc_rows] + child_blocks_at(row_src, row_has, prow_src, prow_has)
    )
    corner_x = spread(mask_all[piv_arr[:2]][:, piv_arr[2:]]) * (
        col_payload[loc_rows:, : 2 * BS] + child_blocks_at(prow_src[:2], prow_has[:2], prow_src[2:], prow_has[2:])
    )
    corner_y = spread(mask_all[piv_arr[2:]][:, piv_arr[:2]]) * (
        col_payload[loc_rows:, 2 * BS:] + child_blocks_at(prow_src[2:], prow_has[2:], prow_src[:2], prow_has[:2])
    )

    alive0_rows = jnp.repeat(lax.dynamic_slice_in_dim(alive0, row_id * row_blocks, row_blocks), BS)
    alive1_rows = jnp.repeat(lax.dynamic_slice_in_dim(alive1, row_id * row_blocks, row_blocks), BS)
    alive0_cb = lax.dynamic_slice_in_dim(alive0, col_id * col_blocks, col_blocks)
    alive1_cb = lax.dynamic_slice_in_dim(alive1, col_id * col_blocks, col_blocks)
    alive0_cols = jnp.repeat(alive0_cb, BS)
    alive1_cols = jnp.repeat(alive1_cb, BS)

    lower0 = dot(col_panels[:, : 2 * BS], diag_inverse[0, 0])
    w0 = lower0 * alive0_rows[:, None]
    mask_rows_p1q1 = lax.dynamic_slice_in_dim(
        jnp.stack([mask_all[:, piv[2]], mask_all[:, piv[3]]], axis=1), row_id * row_blocks, row_blocks, 0
    )
    cp1 = col_panels[:, 2 * BS:] - dot(w0, corner_x) * spread(mask_rows_p1q1)
    lower1 = dot(cp1, diag_inverse[0, 1])
    w1 = lower1 * alive1_rows[:, None]
    rp0 = row_panels[: 2 * BS]
    lower0_p1q1 = dot(corner_y, diag_inverse[0, 0])
    mask_p1q1_cols = lax.dynamic_slice_in_dim(
        jnp.stack([mask_all[piv[2]], mask_all[piv[3]]], axis=0), col_id * col_blocks, col_blocks, 1
    )
    rp1 = row_panels[2 * BS:] - dot(lower0_p1q1, rp0) * spread(mask_p1q1_cols * alive0_cb[None, :])

    lowers = jnp.concatenate([w0, w1], axis=1)
    uppers = jnp.concatenate([rp0 * alive0_cols[None, :], rp1 * alive1_cols[None, :]], axis=0)
    update = dot(lowers, uppers)
    fresh = assembled - update * spread(mask_local)

    lower_blocks = jnp.stack([lower0[:, :BS], lower0[:, BS:], lower1[:, :BS], lower1[:, BS:]])
    live_blocks = jnp.stack([alive0_rows, alive0_rows, alive1_rows, alive1_rows]) > 0
    local_blk = col_id * col_blocks + jnp.arange(col_blocks, dtype=jnp.int32)
    hits = piv_arr[None, :] == local_blk[:, None]
    which = jnp.sum(jnp.where(hits, jnp.arange(4, dtype=jnp.int32)[None, :], 0), axis=1)
    owned = jnp.any(hits, axis=1)
    take_lower = jnp.concatenate(
        [jnp.broadcast_to((live_blocks[which[j]] & owned[j])[:, None], (loc_rows, BS)) for j in range(col_blocks)],
        axis=1,
    )
    lower_cols = jnp.concatenate([lower_blocks[which[j]] for j in range(col_blocks)], axis=1)
    fresh = jnp.where(take_lower, lower_cols, fresh)
    return fresh[None]


def solution(mesh):
    placed = (
        P("front", "row", "col"),
        P("front", "row", "col"),
        P("front"),
        P("front", None),
        P("front", None, None),
        P("front", None),
        P("front", None, None, None),
    )
    return jax.shard_map(
        body, mesh=mesh, in_specs=placed, out_specs=P("front", "row", "col"), check_vma=False
    )
```

```python
import jax
import jax.numpy as jnp
from jax import lax
from jax.sharding import PartitionSpec as P

BS = 256


HIGH = lax.Precision.HIGH


def dot(a, b):
    return jnp.dot(a, b, precision=HIGH, preferred_element_type=jnp.float32)


def body(front_orig, children, parent_of, child_map, block_mask, pivot, diag_inverse):
    row_count = lax.axis_size("row")
    col_count = lax.axis_size("col")
    front_count = lax.axis_size("front")
    row_id = lax.axis_index("row")
    col_id = lax.axis_index("col")
    front_id = lax.axis_index("front")
    matrix_in = front_orig[0]
    loc_rows, loc_cols = matrix_in.shape
    row_blocks = loc_rows // BS
    col_blocks = loc_cols // BS
    kid_rows = children.shape[1] // BS
    kid_cols = children.shape[2] // BS

    def spread(grid):
        r, c = grid.shape
        return jnp.broadcast_to(grid[:, None, :, None], (r, BS, c, BS)).reshape(r * BS, c * BS)

    piece = children[0]
    tags = jnp.concatenate([parent_of, child_map[0]])
    best_piece = jnp.where(tags[0] == front_id, piece, jnp.zeros_like(piece))
    best_tags = jnp.where(tags[0] == front_id, tags, jnp.zeros_like(tags))
    for shift in range(1, front_count):
        perm = [(i, (i + shift) % front_count) for i in range(front_count)]
        got_piece = lax.ppermute(piece, "front", perm)
        got_tags = lax.ppermute(tags, "front", perm)
        hit = got_tags[0] == front_id
        best_piece = jnp.where(hit, got_piece, best_piece)
        best_tags = jnp.where(hit, got_tags, best_tags)
    own_map = best_tags[1:]
    child_blocks = own_map.shape[0]
    block_ranks = jnp.arange(child_blocks, dtype=jnp.int32)

    def locate(first, width):
        target = first + jnp.arange(width, dtype=jnp.int32)
        matches = own_map[:, None] == target[None, :]
        source = jnp.sum(jnp.where(matches, block_ranks[:, None], 0), axis=0)
        return source, jnp.any(matches, axis=0)

    row_src, row_has = locate(row_id * row_blocks, row_blocks)
    col_src, col_has = locate(col_id * col_blocks, col_blocks)
    gathered = lax.all_gather(best_piece, ("row", "col"), axis=0, tiled=False)
    child_tiles = gathered.reshape(row_count, col_count, kid_rows, BS, kid_cols, BS)
    picked = child_tiles[
        (row_src // kid_rows)[:, None],
        (col_src // kid_cols)[None, :],
        (row_src % kid_rows)[:, None],
        :,
        (col_src % kid_cols)[None, :],
        :,
    ]
    keep = row_has[:, None] & col_has[None, :]
    picked = jnp.where(keep[:, :, None, None], picked, 0.0)
    extended = picked.transpose(0, 2, 1, 3).reshape(loc_rows, loc_cols)

    mask_all = block_mask[0].astype(jnp.float32)
    mask_local = lax.dynamic_slice(
        mask_all, (row_id * row_blocks, col_id * col_blocks), (row_blocks, col_blocks)
    )
    assembled = spread(mask_local) * (matrix_in + extended)

    order = pivot[0]
    nblocks = order.shape[0]
    ranks = jnp.arange(nblocks, dtype=jnp.int32)
    position = jnp.sum(jnp.where(order[:, None] == ranks[None, :], ranks[:, None], 0), axis=0)
    alive0 = (position >= 2).astype(jnp.float32)
    alive1 = (position >= 4).astype(jnp.float32)
    piv = [order[k] for k in range(4)]

    def rows_of(blk, mat):
        strip = lax.dynamic_slice_in_dim(mat, (blk % row_blocks) * BS, BS, 0)
        return jnp.where(row_id == blk // row_blocks, strip, 0.0)

    def xor_perm(n, bit):
        return [(i, i ^ bit) for i in range(n)]

    f_rows = jnp.concatenate([rows_of(blk, matrix_in) for blk in piv], axis=0)
    f_rows = f_rows + lax.ppermute(f_rows, "row", xor_perm(row_count, 1))
    half = f_rows.shape[0] // 2
    core = row_id % 2
    mine = jnp.where(core == 0, f_rows[:half], f_rows[half:])
    mine = mine + lax.ppermute(mine, "row", xor_perm(row_count, 2))
    other = lax.ppermute(mine, "row", xor_perm(row_count, 1))
    f_rows = jnp.where(core == 0, jnp.concatenate([mine, other], axis=0), jnp.concatenate([other, mine], axis=0))

    piv_arr = jnp.stack(piv)
    pmatch = own_map[:, None] == piv_arr[None, :]
    prow_src = jnp.sum(jnp.where(pmatch, block_ranks[:, None], 0), axis=0)
    prow_has = jnp.any(pmatch, axis=0)
    picked_rows = child_tiles[
        (prow_src // kid_rows)[:, None],
        (col_src // kid_cols)[None, :],
        (prow_src % kid_rows)[:, None],
        :,
        (col_src % kid_cols)[None, :],
        :,
    ]
    keep_rows = prow_has[:, None] & col_has[None, :]
    picked_rows = jnp.where(keep_rows[:, :, None, None], picked_rows, 0.0)
    placed_rows = picked_rows.transpose(0, 2, 1, 3).reshape(4 * BS, loc_cols)
    mask_piv_rows = lax.dynamic_slice_in_dim(mask_all[piv_arr], col_id * col_blocks, col_blocks, 1)
    row_panels = spread(mask_piv_rows) * (f_rows + placed_rows)

    def cols_of(blk, mat):
        strip = lax.dynamic_slice_in_dim(mat, (blk % col_blocks) * BS, BS, 1)
        return jnp.where(col_id == blk // col_blocks, strip, 0.0)

    f_x = jnp.concatenate([cols_of(piv[2], f_rows[: 2 * BS]), cols_of(piv[3], f_rows[: 2 * BS])], axis=1)
    f_y = jnp.concatenate([cols_of(piv[0], f_rows[2 * BS:]), cols_of(piv[1], f_rows[2 * BS:])], axis=1)
    col_payload = jnp.concatenate(
        [jnp.concatenate([cols_of(blk, matrix_in) for blk in piv], axis=1), jnp.concatenate([f_x, f_y], axis=1)],
        axis=0,
    )
    col_payload = lax.psum(col_payload, "col")

    def child_blocks_at(rsrc, rhas, csrc, chas):
        got = child_tiles[
            (rsrc // kid_rows)[:, None],
            (csrc // kid_cols)[None, :],
            (rsrc % kid_rows)[:, None],
            :,
            (csrc % kid_cols)[None, :],
            :,
        ]
        got = jnp.where((rhas[:, None] & chas[None, :])[:, :, None, None], got, 0.0)
        nr, nc = got.shape[0], got.shape[1]
        return got.transpose(0, 2, 1, 3).reshape(nr * BS, nc * BS)

    mask_rows_local = lax.dynamic_slice_in_dim(mask_all, row_id * row_blocks, row_blocks, 0)
    child_cp, child_x, child_y = lax.optimization_barrier((
        child_blocks_at(row_src, row_has, prow_src, prow_has),
        child_blocks_at(prow_src[:2], prow_has[:2], prow_src[2:], prow_has[2:]),
        child_blocks_at(prow_src[2:], prow_has[2:], prow_src[:2], prow_has[:2]),
    ))
    col_panels = spread(mask_rows_local[:, piv_arr]) * (col_payload[:loc_rows] + child_cp)
    corner_x = spread(mask_all[piv_arr[:2]][:, piv_arr[2:]]) * (
        col_payload[loc_rows:, : 2 * BS] + child_x
    )
    corner_y = spread(mask_all[piv_arr[2:]][:, piv_arr[:2]]) * (
        col_payload[loc_rows:, 2 * BS:] + child_y
    )

    alive0_rows = jnp.repeat(lax.dynamic_slice_in_dim(alive0, row_id * row_blocks, row_blocks), BS)
    alive1_rows = jnp.repeat(lax.dynamic_slice_in_dim(alive1, row_id * row_blocks, row_blocks), BS)
    alive0_cb = lax.dynamic_slice_in_dim(alive0, col_id * col_blocks, col_blocks)
    alive1_cb = lax.dynamic_slice_in_dim(alive1, col_id * col_blocks, col_blocks)
    alive0_cols = jnp.repeat(alive0_cb, BS)
    alive1_cols = jnp.repeat(alive1_cb, BS)

    lower0 = dot(col_panels[:, : 2 * BS], diag_inverse[0, 0])
    w0 = lower0 * alive0_rows[:, None]
    mask_rows_p1q1 = lax.dynamic_slice_in_dim(
        jnp.stack([mask_all[:, piv[2]], mask_all[:, piv[3]]], axis=1), row_id * row_blocks, row_blocks, 0
    )
    cp1 = col_panels[:, 2 * BS:] - dot(w0, corner_x) * spread(mask_rows_p1q1)
    lower1 = dot(cp1, diag_inverse[0, 1])
    w1 = lower1 * alive1_rows[:, None]
    rp0 = row_panels[: 2 * BS]
    lower0_p1q1 = dot(corner_y, diag_inverse[0, 0])
    mask_p1q1_cols = lax.dynamic_slice_in_dim(
        jnp.stack([mask_all[piv[2]], mask_all[piv[3]]], axis=0), col_id * col_blocks, col_blocks, 1
    )
    rp1 = row_panels[2 * BS:] - dot(lower0_p1q1, rp0) * spread(mask_p1q1_cols * alive0_cb[None, :])

    lowers = jnp.concatenate([w0, w1], axis=1)
    uppers = jnp.concatenate([rp0 * alive0_cols[None, :], rp1 * alive1_cols[None, :]], axis=0)
    update = dot(lowers, uppers)
    fresh = assembled - update * spread(mask_local)

    lower_blocks = jnp.stack([lower0[:, :BS], lower0[:, BS:], lower1[:, :BS], lower1[:, BS:]])
    live_blocks = jnp.stack([alive0_rows, alive0_rows, alive1_rows, alive1_rows]) > 0
    local_blk = col_id * col_blocks + jnp.arange(col_blocks, dtype=jnp.int32)
    hits = piv_arr[None, :] == local_blk[:, None]
    which = jnp.sum(jnp.where(hits, jnp.arange(4, dtype=jnp.int32)[None, :], 0), axis=1)
    owned = jnp.any(hits, axis=1)
    take_lower = jnp.concatenate(
        [jnp.broadcast_to((live_blocks[which[j]] & owned[j])[:, None], (loc_rows, BS)) for j in range(col_blocks)],
        axis=1,
    )
    lower_cols = jnp.concatenate([lower_blocks[which[j]] for j in range(col_blocks)], axis=1)
    fresh = jnp.where(take_lower, lower_cols, fresh)
    return fresh[None]


def solution(mesh):
    placed = (
        P("front", "row", "col"),
        P("front", "row", "col"),
        P("front"),
        P("front", None),
        P("front", None, None),
        P("front", None),
        P("front", None, None, None),
    )
    return jax.shard_map(
        body, mesh=mesh, in_specs=placed, out_specs=P("front", "row", "col"), check_vma=False
    )
```
